32 devices in a mesh: grid: 8 (over y, x, core), band: 4 (over z).
Axes of the slice: x: 2, y: 2, z: 4, core: 2. Of those that a mesh axis runs over, the one named last changes fastest.
Arguments:
- occupied: bfloat16 [1024, 32, 24, 128], P('band', 'grid'), may hold values from -6 to 6
- potential: float32 [32, 24, 128], P('grid'), may hold values from 0.2 to 4
- shifts: float32 [64], P('band'), may hold values from 0.5 to 4
- source_term: float32 [64, 32, 24, 128], P('band', 'grid'), may hold values from -125 to 125
Outputs:
- solution: float32 [64, 32, 24, 128], P('band', 'grid')
- residual: float32 [64, 32, 24, 128], P('band', 'grid')
The draws below stay inside these ranges and needn't reach their ends.
All inputs are finite; a program needn't handle non-finite values.
Results may differ from the reference program's by a relative error of at most 0.022.
Values may be sent and summed in bfloat16 or wider, within the bound.
No kernel may reach another device: no remote copies, remote signals or barrier semaphores. Data moves between devices by JAX's collectives and lax.ppermute only.
A program may use at most 128 MiB of HBM per device.

```python
import math
import jax
import jax.numpy as jnp
from jax import lax

OCC = 1024
RESP = 64
NY = 24
NZ = 128
ITERS = 2
NX = 32
N_BAND = 4


def draw_source_term(key, part):
    key_base, key_scale, key_cells = jax.random.split(key, 3)
    position = jnp.arange(NX, dtype=jnp.float32) / max(NX - 1, 1)
    base_values = jax.random.truncated_normal(key_base, -4.0, 4.0, (RESP, NX, NY, NZ), jnp.float32)
    band_scale = jnp.exp(jax.random.uniform(key_scale, (RESP, 1, 1, 1), jnp.float32) * math.log(10.0))
    rise_factor = jnp.exp(position * math.log(3.0))
    cell_scale = jnp.exp(jax.random.uniform(key_cells, (1, NX, NY, NZ), jnp.float32) * math.log(3.3))
    return 0.1 * base_values * band_scale * cell_scale * rise_factor[None, :, None, None]


def shard_levels(rng, dims, cuts, least, high):
    gain, own = 1.0, jax.random.fold_in(rng, 6)
    for axis_at, parts in cuts:
        heights = jnp.exp(jax.random.uniform(jax.random.fold_in(own, axis_at), (parts,), jnp.float32, least / len(cuts), high / len(cuts)))
        gain = gain * jnp.repeat(heights, dims[axis_at] // parts).reshape([-1 if axis == axis_at else 1 for axis in range(len(dims))])
    return gain


def scatter_about(own_key, shape, scale, limit, cuts=(), kind=jnp.bfloat16):
    level = shard_levels(own_key, shape, cuts, -0.22, 0.18) if cuts else 1.0
    drawn = jax.random.normal(own_key, shape, jnp.float32) * scale * level
    return jnp.minimum(jnp.maximum(drawn, -limit), limit).astype(kind)


def setup_inputs(seed: int = 0) -> dict:
    arg_keys = jax.random.split(jax.random.key(seed), 5)
    occupied = scatter_about(arg_keys[0], (OCC, NX, NY, NZ), 1.0, 6.0, ((0, 4), (1, 8)))
    potential = jnp.clip(jnp.exp(math.log(4.0) - 2.9957323 * jax.random.uniform(arg_keys[1], (NX, NY, NZ), jnp.float32) ** shard_levels(arg_keys[1], (NX, NY, NZ), ((0, 8),), -0.2, 0.2)), 0.2, 4.0)
    shifts = jnp.clip(jnp.exp(math.log(4.0) - 2.0794415 * jax.random.uniform(arg_keys[2], (RESP,), jnp.float32) ** shard_levels(arg_keys[2], (RESP,), ((0, 4),), -0.2, 0.2)), 0.5, 4.0)
    source_term = draw_source_term(jax.random.fold_in(arg_keys[4], 71), 0)
    return {"occupied": occupied, "potential": potential, "shifts": shifts, "source_term": source_term}


COEFFICIENTS = (-205.0 / 72.0, 8.0 / 5.0, -1.0 / 5.0, 8.0 / 315.0, -1.0 / 560.0)

def second_sum(padded, extent_x, extent_y, extent_z):
    middle = padded[:, 4:4 + extent_x, 4:4 + extent_y, 4:4 + extent_z]
    summed = 3.0 * COEFFICIENTS[0] * middle
    for offset in range(1, 5):
        along_x = padded[:, 4 + offset:4 + offset + extent_x, 4:4 + extent_y, 4:4 + extent_z] + padded[:, 4 - offset:4 - offset + extent_x, 4:4 + extent_y, 4:4 + extent_z]
        along_y = padded[:, 4:4 + extent_x, 4 + offset:4 + offset + extent_y, 4:4 + extent_z] + padded[:, 4:4 + extent_x, 4 - offset:4 - offset + extent_y, 4:4 + extent_z]
        along_z = padded[:, 4:4 + extent_x, 4:4 + extent_y, 4 + offset:4 + offset + extent_z] + padded[:, 4:4 + extent_x, 4:4 + extent_y, 4 - offset:4 - offset + extent_z]
        summed = summed + COEFFICIENTS[offset] * along_x + COEFFICIENTS[offset] * along_y + COEFFICIENTS[offset] * along_z
    return summed

def project(direction, occupied):
    band_total = direction.shape[0]
    occupied_total = occupied.shape[0]
    cell_total = direction.shape[1] * direction.shape[2] * direction.shape[3]
    weight_scale = 2.0 / math.sqrt(occupied_total * cell_total)
    rounded = direction.astype(jnp.bfloat16).reshape(band_total, cell_total).astype(jnp.float32)
    groups = occupied.reshape(N_BAND, occupied_total // N_BAND, cell_total)

    def margin(group_rows):
        return lax.dot_general(group_rows.astype(jnp.float32), rounded, (((1,), (1,)), ((), ())), precision=lax.Precision.HIGHEST)
    margins = lax.map(margin, groups)
    scaled = (margins * weight_scale).astype(jnp.bfloat16)

    def add_group(running, member_pair):
        coefficients_group, group_rows = member_pair
        group_term = lax.dot_general(coefficients_group.astype(jnp.float32), group_rows.astype(jnp.float32), (((0,), (0,)), ((), ())), precision=lax.Precision.HIGHEST)
        group_term = lax.optimization_barrier(group_term.astype(jnp.bfloat16)).astype(jnp.float32)
        return (running + group_term, None)
    summed, unused = lax.scan(add_group, jnp.zeros((band_total, cell_total), jnp.float32), (scaled, groups))
    return summed.reshape(direction.shape)

def apply_operator(direction, occupied, potential, shifts):
    extent_x, extent_y, extent_z = (direction.shape[1], direction.shape[2], direction.shape[3])
    padded = jnp.pad(direction, ((0, 0), (4, 4), (4, 4), (4, 4)))
    kinetic = -0.5 * second_sum(padded, extent_x, extent_y, extent_z)
    local_part = kinetic + (potential[None] + shifts[:, None, None, None]) * direction
    return local_part + project(direction, occupied)

def inner_product(first_field, second_field):
    return lax.optimization_barrier(jnp.sum(first_field * second_field, axis=(1, 2, 3)))

def expand(vector):
    return vector[:, None, None, None]

def reference(occupied, potential, shifts, source_term):
    solution = jnp.zeros_like(source_term)
    residual = source_term
    direction = source_term
    norm_now = inner_product(residual, residual)
    for iteration in range(ITERS):
        applied = apply_operator(direction, occupied, potential, shifts)
        step_size = norm_now / inner_product(direction, applied)
        solution = solution + expand(step_size) * direction
        residual = residual - expand(step_size) * applied
        if iteration + 1 < ITERS:
            norm_next = inner_product(residual, residual)
            direction = residual + expand(norm_next / norm_now) * direction
            norm_now = norm_next
    return (solution, residual)
```

```python
import math

import jax
import jax.numpy as jnp
from jax import lax
from jax.sharding import PartitionSpec as P

ITERS = 2


COEFFICIENTS = (-205.0 / 72.0, 8.0 / 5.0, -1.0 / 5.0, 8.0 / 315.0, -1.0 / 560.0)


def with_halo(shard, sides, width):
    for axis, dim in sides:
        peers, length = (lax.axis_size(axis), shard.shape[dim])
        up = [(i, (i + 1) % peers) for i in range(peers - 1)]
        down = [(j, i) for i, j in up]
        last = lax.slice_in_dim(shard, length - width, length, axis=dim)
        leading = lax.slice_in_dim(shard, 0, width, axis=dim)
        before = lax.ppermute(last, axis, up)
        after = lax.ppermute(leading, axis, down)
        shard = jnp.concatenate([before, shard, after], axis=dim)
    return shard


def grid_sum(value, axis):
    peers = lax.axis_size(axis)
    assert peers & (peers - 1) == 0
    stride = 1
    while stride < peers:
        pairs = [(i, i ^ stride) for i in range(peers)]
        value = value + lax.ppermute(value, axis, pairs)
        stride *= 2
    return value


def second_sum(padded, extent_x, extent_y, extent_z):
    middle = padded[:, 4 : 4 + extent_x, 4 : 4 + extent_y, 4 : 4 + extent_z]
    summed = 3.0 * COEFFICIENTS[0] * middle
    for offset in range(1, 5):
        along_x = (
            padded[:, 4 + offset : 4 + offset + extent_x, 4 : 4 + extent_y, 4 : 4 + extent_z]
            + padded[:, 4 - offset : 4 - offset + extent_x, 4 : 4 + extent_y, 4 : 4 + extent_z]
        )
        along_y = (
            padded[:, 4 : 4 + extent_x, 4 + offset : 4 + offset + extent_y, 4 : 4 + extent_z]
            + padded[:, 4 : 4 + extent_x, 4 - offset : 4 - offset + extent_y, 4 : 4 + extent_z]
        )
        along_z = (
            padded[:, 4 : 4 + extent_x, 4 : 4 + extent_y, 4 + offset : 4 + offset + extent_z]
            + padded[:, 4 : 4 + extent_x, 4 : 4 + extent_y, 4 - offset : 4 - offset + extent_z]
        )
        summed = (
            summed
            + COEFFICIENTS[offset] * along_x
            + COEFFICIENTS[offset] * along_y
            + COEFFICIENTS[offset] * along_z
        )
    return summed


def inner_product(first_field, second_field):
    return jnp.sum(first_field * second_field, axis=(1, 2, 3))


def expand(vector):
    return vector[:, None, None, None]


def body(occupied, potential, shifts, source_term):
    local_bands, width_x, width_y, width_z = source_term.shape
    local_occupied = occupied.shape[0]
    band_count = lax.axis_size("band")
    local_cells = width_x * width_y * width_z
    weight_scale = 2.0 / math.sqrt(
        local_occupied * band_count * local_cells * lax.axis_size("grid")
    )
    occupied_rows = occupied.reshape(local_occupied, local_cells)
    potential_shift = potential[None] + shifts[:, None, None, None]
    solution = jnp.zeros_like(source_term)
    residual = source_term
    direction = source_term
    norm_now = grid_sum(inner_product(source_term, source_term), "grid")
    for iteration in range(ITERS):
        padded = with_halo(direction.astype(jnp.bfloat16), (("grid", 1),), 4).astype(
            direction.dtype
        )
        padded = jnp.pad(padded, ((0, 0), (0, 0), (4, 4), (4, 4)))
        kinetic = -0.5 * second_sum(padded, width_x, width_y, width_z)
        rounded = direction.astype(jnp.bfloat16).reshape(local_bands, local_cells)
        partial_margin = lax.dot_general(
            occupied_rows,
            lax.all_gather(rounded, "band", axis=0, tiled=True),
            (((1,), (1,)), ((), ())),
            preferred_element_type=jnp.float32,
        )
        margins = grid_sum(partial_margin, "grid")
        scaled = (margins * weight_scale).astype(jnp.bfloat16)
        projected = lax.psum_scatter(
            lax.dot_general(
                scaled, occupied_rows, (((0,), (0,)), ((), ())), preferred_element_type=jnp.float32
            ).astype(jnp.bfloat16),
            "band",
            scatter_dimension=0,
            tiled=True,
        ).astype(jnp.float32)
        applied = kinetic + potential_shift * direction + projected.reshape(direction.shape)
        curvature = grid_sum(inner_product(direction, applied), "grid")
        step_size = norm_now / curvature
        solution = solution + expand(step_size) * direction
        residual = residual - expand(step_size) * applied
        if iteration + 1 < ITERS:
            norm_next = grid_sum(inner_product(residual, residual), "grid")
            direction = residual + expand(norm_next / norm_now) * direction
            norm_now = norm_next
    return (solution, residual)


def solution(mesh):
    in_specs = (
        P("band", "grid", None, None),
        P("grid", None, None),
        P("band"),
        P("band", "grid", None, None),
    )
    out_specs = (P("band", "grid", None, None), P("band", "grid", None, None))
    return jax.shard_map(body, mesh=mesh, in_specs=in_specs, out_specs=out_specs, check_vma=False)
```

```python
import math

import jax
import jax.numpy as jnp
from jax import lax
from jax.sharding import PartitionSpec as P

ITERS = 2


COEFFICIENTS = (-205.0 / 72.0, 8.0 / 5.0, -1.0 / 5.0, 8.0 / 315.0, -1.0 / 560.0)


def with_halo(shard, sides, width):
    for axis, dim in sides:
        peers, length = (lax.axis_size(axis), shard.shape[dim])
        up = [(i, (i + 1) % peers) for i in range(peers - 1)]
        down = [(j, i) for i, j in up]
        last = lax.slice_in_dim(shard, length - width, length, axis=dim)
        leading = lax.slice_in_dim(shard, 0, width, axis=dim)
        before = lax.ppermute(last, axis, up)
        after = lax.ppermute(leading, axis, down)
        shard = jnp.concatenate([before, shard, after], axis=dim)
    return shard


def grid_sum(value, axis):
    peers = lax.axis_size(axis)
    assert peers & (peers - 1) == 0
    stride = 1
    while stride < peers:
        pairs = [(i, i ^ stride) for i in range(peers)]
        value = value + lax.ppermute(value, axis, pairs)
        stride *= 2
    return value


def second_sum(padded, extent_x, extent_y, extent_z):
    middle = padded[:, 4 : 4 + extent_x, 4 : 4 + extent_y, 4 : 4 + extent_z]
    summed = 3.0 * COEFFICIENTS[0] * middle
    for offset in range(1, 5):
        along_x = (
            padded[:, 4 + offset : 4 + offset + extent_x, 4 : 4 + extent_y, 4 : 4 + extent_z]
            + padded[:, 4 - offset : 4 - offset + extent_x, 4 : 4 + extent_y, 4 : 4 + extent_z]
        )
        along_y = (
            padded[:, 4 : 4 + extent_x, 4 + offset : 4 + offset + extent_y, 4 : 4 + extent_z]
            + padded[:, 4 : 4 + extent_x, 4 - offset : 4 - offset + extent_y, 4 : 4 + extent_z]
        )
        along_z = (
            padded[:, 4 : 4 + extent_x, 4 : 4 + extent_y, 4 + offset : 4 + offset + extent_z]
            + padded[:, 4 : 4 + extent_x, 4 : 4 + extent_y, 4 - offset : 4 - offset + extent_z]
        )
        summed = (
            summed
            + COEFFICIENTS[offset] * along_x
            + COEFFICIENTS[offset] * along_y
            + COEFFICIENTS[offset] * along_z
        )
    return summed


def inner_product(first_field, second_field):
    return jnp.sum(first_field * second_field, axis=(1, 2, 3))


def expand(vector):
    return vector[:, None, None, None]


def body(occupied, potential, shifts, source_term):
    local_bands, width_x, width_y, width_z = source_term.shape
    local_occupied = occupied.shape[0]
    band_count = lax.axis_size("band")
    local_cells = width_x * width_y * width_z
    weight_scale = 2.0 / math.sqrt(
        local_occupied * band_count * local_cells * lax.axis_size("grid")
    )
    occupied_rows = occupied.reshape(local_occupied, local_cells)
    potential_shift = potential[None] + shifts[:, None, None, None]
    solution = jnp.zeros_like(source_term)
    residual = source_term
    direction = source_term
    norm_now = grid_sum(inner_product(source_term, source_term), "grid")
    for iteration in range(ITERS):
        padded = with_halo(direction.astype(jnp.bfloat16), (("grid", 1),), 4).astype(
            direction.dtype
        )
        padded = jnp.pad(padded, ((0, 0), (0, 0), (4, 4), (4, 4)))
        kinetic = -0.5 * second_sum(padded, width_x, width_y, width_z)
        rounded = direction.astype(jnp.bfloat16).reshape(local_bands, local_cells)
        blocks = [rounded] + [
            lax.ppermute(rounded, "band", [(i, (i + d) % band_count) for i in range(band_count)])
            for d in range(1, band_count)
        ]
        gathered = jnp.concatenate(blocks, axis=0)
        partial_margin = lax.dot_general(
            occupied_rows, gathered, (((1,), (1,)), ((), ())), preferred_element_type=jnp.float32
        )
        margins = grid_sum(partial_margin, "grid")
        scaled = (margins * weight_scale).astype(jnp.bfloat16)
        terms = lax.dot_general(
            scaled, occupied_rows, (((0,), (0,)), ((), ())), preferred_element_type=jnp.float32
        ).astype(jnp.bfloat16)
        projected = terms[:local_bands].astype(jnp.float32)
        for d in range(1, band_count):
            part = terms[d * local_bands : (d + 1) * local_bands]
            back = lax.ppermute(part, "band", [((i + d) % band_count, i) for i in range(band_count)])
            projected = projected + back.astype(jnp.float32)
        applied = kinetic + potential_shift * direction + projected.reshape(direction.shape)
        curvature = grid_sum(inner_product(direction, applied), "grid")
        step_size = norm_now / curvature
        solution = solution + expand(step_size) * direction
        residual = residual - expand(step_size) * applied
        if iteration + 1 < ITERS:
            norm_next = grid_sum(inner_product(residual, residual), "grid")
            direction = residual + expand(norm_next / norm_now) * direction
            norm_now = norm_next
    return (solution, residual)


def solution(mesh):
    in_specs = (
        P("band", "grid", None, None),
        P("grid", None, None),
        P("band"),
        P("band", "grid", None, None),
    )
    out_specs = (P("band", "grid", None, None), P("band", "grid", None, None))
    return jax.shard_map(body, mesh=mesh, in_specs=in_specs, out_specs=out_specs, check_vma=False)
```

```python
import math

import jax
import jax.numpy as jnp
from jax import lax
from jax.sharding import PartitionSpec as P

ITERS = 2


COEFFICIENTS = (-205.0 / 72.0, 8.0 / 5.0, -1.0 / 5.0, 8.0 / 315.0, -1.0 / 560.0)


def with_halo(shard, sides, width):
    for axis, dim in sides:
        peers, length = (lax.axis_size(axis), shard.shape[dim])
        up = [(i, (i + 1) % peers) for i in range(peers - 1)]
        down = [(j, i) for i, j in up]
        last = lax.slice_in_dim(shard, length - width, length, axis=dim)
        leading = lax.slice_in_dim(shard, 0, width, axis=dim)
        before = lax.ppermute(last, axis, up)
        after = lax.ppermute(leading, axis, down)
        shard = jnp.concatenate([before, shard, after], axis=dim)
    return shard


def grid_sum(value, axis):
    peers = lax.axis_size(axis)
    assert peers & (peers - 1) == 0
    stride = 1
    while stride < peers:
        radix = min(8, peers // stride)
        total = value
        for k in range(1, radix):
            pairs = [(i, i ^ (k * stride)) for i in range(peers)]
            total = total + lax.ppermute(value, axis, pairs)
        value = total
        stride *= radix
    return value


def second_sum(padded, extent_x, extent_y, extent_z):
    middle = padded[:, 4 : 4 + extent_x, 4 : 4 + extent_y, 4 : 4 + extent_z]
    summed = 3.0 * COEFFICIENTS[0] * middle
    for offset in range(1, 5):
        along_x = (
            padded[:, 4 + offset : 4 + offset + extent_x, 4 : 4 + extent_y, 4 : 4 + extent_z]
            + padded[:, 4 - offset : 4 - offset + extent_x, 4 : 4 + extent_y, 4 : 4 + extent_z]
        )
        along_y = (
            padded[:, 4 : 4 + extent_x, 4 + offset : 4 + offset + extent_y, 4 : 4 + extent_z]
            + padded[:, 4 : 4 + extent_x, 4 - offset : 4 - offset + extent_y, 4 : 4 + extent_z]
        )
        along_z = (
            padded[:, 4 : 4 + extent_x, 4 : 4 + extent_y, 4 + offset : 4 + offset + extent_z]
            + padded[:, 4 : 4 + extent_x, 4 : 4 + extent_y, 4 - offset : 4 - offset + extent_z]
        )
        summed = (
            summed
            + COEFFICIENTS[offset] * along_x
            + COEFFICIENTS[offset] * along_y
            + COEFFICIENTS[offset] * along_z
        )
    return summed


def inner_product(first_field, second_field):
    return jnp.sum(first_field * second_field, axis=(1, 2, 3))


def expand(vector):
    return vector[:, None, None, None]


def body(occupied, potential, shifts, source_term):
    local_bands, width_x, width_y, width_z = source_term.shape
    local_occupied = occupied.shape[0]
    band_count = lax.axis_size("band")
    local_cells = width_x * width_y * width_z
    weight_scale = 2.0 / math.sqrt(
        local_occupied * band_count * local_cells * lax.axis_size("grid")
    )
    occupied_rows = occupied.reshape(local_occupied, local_cells)
    potential_shift = potential[None] + shifts[:, None, None, None]
    solution = jnp.zeros_like(source_term)
    residual = source_term
    direction = source_term
    norm_now = grid_sum(inner_product(source_term, source_term), "grid")
    for iteration in range(ITERS):
        padded = with_halo(direction.astype(jnp.bfloat16), (("grid", 1),), 4).astype(
            direction.dtype
        )
        padded = jnp.pad(padded, ((0, 0), (0, 0), (4, 4), (4, 4)))
        kinetic = -0.5 * second_sum(padded, width_x, width_y, width_z)
        rounded = direction.astype(jnp.bfloat16).reshape(local_bands, local_cells)
        blocks = [rounded] + [
            lax.ppermute(rounded, "band", [(i, (i + d) % band_count) for i in range(band_count)])
            for d in range(1, band_count)
        ]
        partial_margin = jnp.concatenate(
            [
                lax.dot_general(
                    occupied_rows, block, (((1,), (1,)), ((), ())), preferred_element_type=jnp.float32
                )
                for block in blocks
            ],
            axis=1,
        )
        margins = grid_sum(partial_margin, "grid")
        scaled = (margins * weight_scale).astype(jnp.bfloat16)
        projected = None
        for d in range(band_count):
            part = lax.dot_general(
                scaled[:, d * local_bands : (d + 1) * local_bands],
                occupied_rows,
                (((0,), (0,)), ((), ())),
                preferred_element_type=jnp.float32,
            ).astype(jnp.bfloat16)
            if d:
                part = lax.ppermute(part, "band", [((i + d) % band_count, i) for i in range(band_count)])
            part = part.astype(jnp.float32)
            projected = part if projected is None else projected + part
        applied = kinetic + potential_shift * direction + projected.reshape(direction.shape)
        curvature = grid_sum(inner_product(direction, applied), "grid")
        step_size = norm_now / curvature
        solution = solution + expand(step_size) * direction
        residual = residual - expand(step_size) * applied
        if iteration + 1 < ITERS:
            norm_next = grid_sum(inner_product(residual, residual), "grid")
            direction = residual + expand(norm_next / norm_now) * direction
            norm_now = norm_next
    return (solution, residual)


def solution(mesh):
    in_specs = (
        P("band", "grid", None, None),
        P("grid", None, None),
        P("band"),
        P("band", "grid", None, None),
    )
    out_specs = (P("band", "grid", None, None), P("band", "grid", None, None))
    return jax.shard_map(body, mesh=mesh, in_specs=in_specs, out_specs=out_specs, check_vma=False)
```

```python
import math

import jax
import jax.numpy as jnp
from jax import lax
from jax.sharding import PartitionSpec as P

ITERS = 2


COEFFICIENTS = (-205.0 / 72.0, 8.0 / 5.0, -1.0 / 5.0, 8.0 / 315.0, -1.0 / 560.0)


def with_halo(shard, sides, width):
    for axis, dim in sides:
        peers, length = (lax.axis_size(axis), shard.shape[dim])
        up = [(i, (i + 1) % peers) for i in range(peers - 1)]
        down = [(j, i) for i, j in up]
        last = lax.slice_in_dim(shard, length - width, length, axis=dim)
        leading = lax.slice_in_dim(shard, 0, width, axis=dim)
        before = lax.ppermute(last, axis, up)
        after = lax.ppermute(leading, axis, down)
        shard = jnp.concatenate([before, shard, after], axis=dim)
    return shard


def grid_sum(value, axis):
    peers = lax.axis_size(axis)
    assert peers & (peers - 1) == 0
    stride = 1
    while stride < peers:
        pairs = [(i, i ^ stride) for i in range(peers)]
        value = value + lax.ppermute(value, axis, pairs)
        stride *= 2
    return value


def second_sum(padded, extent_x, extent_y, extent_z):
    middle = padded[:, 4 : 4 + extent_x, 4 : 4 + extent_y, 4 : 4 + extent_z]
    summed = 3.0 * COEFFICIENTS[0] * middle
    for offset in range(1, 5):
        along_x = (
            padded[:, 4 + offset : 4 + offset + extent_x, 4 : 4 + extent_y, 4 : 4 + extent_z]
            + padded[:, 4 - offset : 4 - offset + extent_x, 4 : 4 + extent_y, 4 : 4 + extent_z]
        )
        along_y = (
            padded[:, 4 : 4 + extent_x, 4 + offset : 4 + offset + extent_y, 4 : 4 + extent_z]
            + padded[:, 4 : 4 + extent_x, 4 - offset : 4 - offset + extent_y, 4 : 4 + extent_z]
        )
        along_z = (
            padded[:, 4 : 4 + extent_x, 4 : 4 + extent_y, 4 + offset : 4 + offset + extent_z]
            + padded[:, 4 : 4 + extent_x, 4 : 4 + extent_y, 4 - offset : 4 - offset + extent_z]
        )
        summed = (
            summed
            + COEFFICIENTS[offset] * along_x
            + COEFFICIENTS[offset] * along_y
            + COEFFICIENTS[offset] * along_z
        )
    return summed


def inner_product(first_field, second_field):
    return jnp.sum(first_field * second_field, axis=(1, 2, 3))


def expand(vector):
    return vector[:, None, None, None]


def chain(occupied, potential, shifts, source_term):
    local_bands, width_x, width_y, width_z = source_term.shape
    local_occupied = occupied.shape[0]
    band_count = lax.axis_size("band")
    local_cells = width_x * width_y * width_z
    weight_scale = 2.0 / math.sqrt(
        local_occupied * band_count * local_cells * lax.axis_size("grid")
    )
    occupied_rows = occupied.reshape(local_occupied, local_cells)
    potential_shift = potential[None] + shifts[:, None, None, None]
    solution = jnp.zeros_like(source_term)
    residual = source_term
    direction = source_term
    norm_now = grid_sum(inner_product(source_term, source_term), "grid")
    for iteration in range(ITERS):
        padded = with_halo(direction.astype(jnp.bfloat16), (("grid", 1),), 4).astype(
            direction.dtype
        )
        padded = jnp.pad(padded, ((0, 0), (0, 0), (4, 4), (4, 4)))
        kinetic = -0.5 * second_sum(padded, width_x, width_y, width_z)
        rounded = direction.astype(jnp.bfloat16).reshape(local_bands, local_cells)
        blocks = [rounded] + [
            lax.ppermute(rounded, "band", [(i, (i + d) % band_count) for i in range(band_count)])
            for d in range(1, band_count)
        ]
        gathered = jnp.concatenate(blocks, axis=0)
        partial_margin = lax.dot_general(
            occupied_rows, gathered, (((1,), (1,)), ((), ())), preferred_element_type=jnp.float32
        )
        margins = grid_sum(partial_margin, "grid")
        scaled = (margins * weight_scale).astype(jnp.bfloat16)
        terms = lax.dot_general(
            scaled, occupied_rows, (((0,), (0,)), ((), ())), preferred_element_type=jnp.float32
        ).astype(jnp.bfloat16)
        projected = terms[:local_bands].astype(jnp.float32)
        for d in range(1, band_count):
            part = terms[d * local_bands : (d + 1) * local_bands]
            back = lax.ppermute(part, "band", [((i + d) % band_count, i) for i in range(band_count)])
            projected = projected + back.astype(jnp.float32)
        applied = kinetic + potential_shift * direction + projected.reshape(direction.shape)
        curvature = grid_sum(inner_product(direction, applied), "grid")
        step_size = norm_now / curvature
        solution = solution + expand(step_size) * direction
        residual = residual - expand(step_size) * applied
        if iteration + 1 < ITERS:
            norm_next = grid_sum(inner_product(residual, residual), "grid")
            direction = residual + expand(norm_next / norm_now) * direction
            norm_now = norm_next
    return (solution, residual)


def body(occupied, potential, shifts, source_term):
    pieces = 2 if source_term.shape[0] % 2 == 0 else 1
    width = source_term.shape[0] // pieces
    results = [
        chain(occupied, potential, shifts[k * width : (k + 1) * width], source_term[k * width : (k + 1) * width])
        for k in range(pieces)
    ]
    return tuple(jnp.concatenate([r[i] for r in results], axis=0) for i in range(2))


def solution(mesh):
    in_specs = (
        P("band", "grid", None, None),
        P("grid", None, None),
        P("band"),
        P("band", "grid", None, None),
    )
    out_specs = (P("band", "grid", None, None), P("band", "grid", None, None))
    return jax.shard_map(body, mesh=mesh, in_specs=in_specs, out_specs=out_specs, check_vma=False)
```

```python
import math

import jax
import jax.numpy as jnp
from jax import lax
from jax.sharding import PartitionSpec as P

ITERS = 2


COEFFICIENTS = (-205.0 / 72.0, 8.0 / 5.0, -1.0 / 5.0, 8.0 / 315.0, -1.0 / 560.0)


def with_halo(shard, sides, width):
    for axis, dim in sides:
        peers, length = (lax.axis_size(axis), shard.shape[dim])
        up = [(i, (i + 1) % peers) for i in range(peers - 1)]
        down = [(j, i) for i, j in up]
        last = lax.slice_in_dim(shard, length - width, length, axis=dim)
        leading = lax.slice_in_dim(shard, 0, width, axis=dim)
        before = lax.ppermute(last, axis, up)
        after = lax.ppermute(leading, axis, down)
        shard = jnp.concatenate([before, shard, after], axis=dim)
    return shard


def grid_sum(value, axis):
    peers = lax.axis_size(axis)
    assert peers & (peers - 1) == 0
    stride = 1
    while stride < peers:
        pairs = [(i, i ^ stride) for i in range(peers)]
        value = value + lax.ppermute(value, axis, pairs)
        stride *= 2
    return value


def band_gather(block, peers):
    blocks = [block] + [jnp.zeros_like(block) for _ in range(1, peers)]
    rightward, leftward = block, block
    for s in range(1, peers):
        rightward = lax.ppermute(rightward, "band", [(i, i + 1) for i in range(s - 1, peers - 1)])
        leftward = lax.ppermute(leftward, "band", [(i + 1, i) for i in range(peers - s)])
        blocks[s] = blocks[s] + rightward
        blocks[peers - s] = blocks[peers - s] + leftward
    return blocks


def band_reduce(terms, peers):
    total = terms[0]
    if peers == 1:
        return total
    carry_left = jnp.zeros(terms[0].shape, jnp.bfloat16)
    carry_right = jnp.zeros(terms[0].shape, jnp.bfloat16)
    for s in range(1, peers):
        message = (terms[peers - s] + carry_left.astype(jnp.float32)).astype(jnp.bfloat16)
        carry_left = lax.ppermute(message, "band", [(k, k - 1) for k in range(peers - s, peers)])
        message = (terms[s] + carry_right.astype(jnp.float32)).astype(jnp.bfloat16)
        carry_right = lax.ppermute(message, "band", [(k, k + 1) for k in range(s)])
    return total + carry_left.astype(jnp.float32) + carry_right.astype(jnp.float32)


def second_sum(padded, extent_x, extent_y, extent_z):
    middle = padded[:, 4 : 4 + extent_x, 4 : 4 + extent_y, 4 : 4 + extent_z]
    summed = 3.0 * COEFFICIENTS[0] * middle
    for offset in range(1, 5):
        along_x = (
            padded[:, 4 + offset : 4 + offset + extent_x, 4 : 4 + extent_y, 4 : 4 + extent_z]
            + padded[:, 4 - offset : 4 - offset + extent_x, 4 : 4 + extent_y, 4 : 4 + extent_z]
        )
        along_y = (
            padded[:, 4 : 4 + extent_x, 4 + offset : 4 + offset + extent_y, 4 : 4 + extent_z]
            + padded[:, 4 : 4 + extent_x, 4 - offset : 4 - offset + extent_y, 4 : 4 + extent_z]
        )
        along_z = (
            padded[:, 4 : 4 + extent_x, 4 : 4 + extent_y, 4 + offset : 4 + offset + extent_z]
            + padded[:, 4 : 4 + extent_x, 4 : 4 + extent_y, 4 - offset : 4 - offset + extent_z]
        )
        summed = (
            summed
            + COEFFICIENTS[offset] * along_x
            + COEFFICIENTS[offset] * along_y
            + COEFFICIENTS[offset] * along_z
        )
    return summed


def inner_product(first_field, second_field):
    return jnp.sum(first_field * second_field, axis=(1, 2, 3))


def expand(vector):
    return vector[:, None, None, None]


def chain(occupied, potential, shifts, source_term):
    local_bands, width_x, width_y, width_z = source_term.shape
    local_occupied = occupied.shape[0]
    band_count = lax.axis_size("band")
    local_cells = width_x * width_y * width_z
    weight_scale = 2.0 / math.sqrt(
        local_occupied * band_count * local_cells * lax.axis_size("grid")
    )
    occupied_rows = occupied.reshape(local_occupied, local_cells)
    potential_shift = potential[None] + shifts[:, None, None, None]
    solution = jnp.zeros_like(source_term)
    residual = source_term
    direction = source_term
    norm_now = grid_sum(inner_product(source_term, source_term), "grid")
    for iteration in range(ITERS):
        padded = with_halo(direction.astype(jnp.bfloat16), (("grid", 1),), 4).astype(
            direction.dtype
        )
        padded = jnp.pad(padded, ((0, 0), (0, 0), (4, 4), (4, 4)))
        kinetic = -0.5 * second_sum(padded, width_x, width_y, width_z)
        rounded = direction.astype(jnp.bfloat16).reshape(local_bands, local_cells)
        blocks = band_gather(rounded, band_count)
        gathered = jnp.concatenate(blocks, axis=0)
        partial_margin = lax.dot_general(
            occupied_rows, gathered, (((1,), (1,)), ((), ())), preferred_element_type=jnp.float32
        )
        margins = grid_sum(partial_margin, "grid")
        scaled = (margins * weight_scale).astype(jnp.bfloat16)
        terms = lax.dot_general(
            scaled, occupied_rows, (((0,), (0,)), ((), ())), preferred_element_type=jnp.float32
        )
        projected = band_reduce(
            [terms[d * local_bands : (d + 1) * local_bands] for d in range(band_count)], band_count
        )
        applied = kinetic + potential_shift * direction + projected.reshape(direction.shape)
        curvature = grid_sum(inner_product(direction, applied), "grid")
        step_size = norm_now / curvature
        solution = solution + expand(step_size) * direction
        residual = residual - expand(step_size) * applied
        if iteration + 1 < ITERS:
            norm_next = grid_sum(inner_product(residual, residual), "grid")
            direction = residual + expand(norm_next / norm_now) * direction
            norm_now = norm_next
    return (solution, residual)


def body(occupied, potential, shifts, source_term):
    pieces = 2 if source_term.shape[0] % 2 == 0 else 1
    width = source_term.shape[0] // pieces
    results = [
        chain(occupied, potential, shifts[k * width : (k + 1) * width], source_term[k * width : (k + 1) * width])
        for k in range(pieces)
    ]
    return tuple(jnp.concatenate([r[i] for r in results], axis=0) for i in range(2))


def solution(mesh):
    in_specs = (
        P("band", "grid", None, None),
        P("grid", None, None),
        P("band"),
        P("band", "grid", None, None),
    )
    out_specs = (P("band", "grid", None, None), P("band", "grid", None, None))
    return jax.shard_map(body, mesh=mesh, in_specs=in_specs, out_specs=out_specs, check_vma=False)
```

```python
import math

import jax
import jax.numpy as jnp
from jax import lax
from jax.sharding import PartitionSpec as P

ITERS = 2


COEFFICIENTS = (-205.0 / 72.0, 8.0 / 5.0, -1.0 / 5.0, 8.0 / 315.0, -1.0 / 560.0)


def with_halo(shard, sides, width):
    for axis, dim in sides:
        peers, length = (lax.axis_size(axis), shard.shape[dim])
        up = [(i, (i + 1) % peers) for i in range(peers - 1)]
        down = [(j, i) for i, j in up]
        last = lax.slice_in_dim(shard, length - width, length, axis=dim)
        leading = lax.slice_in_dim(shard, 0, width, axis=dim)
        before = lax.ppermute(last, axis, up)
        after = lax.ppermute(leading, axis, down)
        shard = jnp.concatenate([before, shard, after], axis=dim)
    return shard


def grid_sum(value, axis):
    peers = lax.axis_size(axis)
    assert peers & (peers - 1) == 0
    stride = 1
    while stride < peers:
        pairs = [(i, i ^ stride) for i in range(peers)]
        value = value + lax.ppermute(value, axis, pairs)
        stride *= 2
    return value


def second_sum(padded, extent_x, extent_y, extent_z):
    middle = padded[:, 4 : 4 + extent_x, 4 : 4 + extent_y, 4 : 4 + extent_z]
    summed = 3.0 * COEFFICIENTS[0] * middle
    for offset in range(1, 5):
        along_x = (
            padded[:, 4 + offset : 4 + offset + extent_x, 4 : 4 + extent_y, 4 : 4 + extent_z]
            + padded[:, 4 - offset : 4 - offset + extent_x, 4 : 4 + extent_y, 4 : 4 + extent_z]
        )
        along_y = (
            padded[:, 4 : 4 + extent_x, 4 + offset : 4 + offset + extent_y, 4 : 4 + extent_z]
            + padded[:, 4 : 4 + extent_x, 4 - offset : 4 - offset + extent_y, 4 : 4 + extent_z]
        )
        along_z = (
            padded[:, 4 : 4 + extent_x, 4 : 4 + extent_y, 4 + offset : 4 + offset + extent_z]
            + padded[:, 4 : 4 + extent_x, 4 : 4 + extent_y, 4 - offset : 4 - offset + extent_z]
        )
        summed = (
            summed
            + COEFFICIENTS[offset] * along_x
            + COEFFICIENTS[offset] * along_y
            + COEFFICIENTS[offset] * along_z
        )
    return summed


def inner_product(first_field, second_field):
    return jnp.sum(first_field * second_field, axis=(1, 2, 3))


def expand(vector):
    return vector[:, None, None, None]


def chain(occupied, potential, shifts, source_term):
    local_bands, width_x, width_y, width_z = source_term.shape
    local_occupied = occupied.shape[0]
    band_count = lax.axis_size("band")
    local_cells = width_x * width_y * width_z
    weight_scale = 2.0 / math.sqrt(
        local_occupied * band_count * local_cells * lax.axis_size("grid")
    )
    occupied_rows = occupied.reshape(local_occupied, local_cells)
    potential_shift = potential[None] + shifts[:, None, None, None]
    solution = jnp.zeros_like(source_term)
    residual = source_term
    direction = source_term
    norm_now = grid_sum(inner_product(source_term, source_term), "grid")
    for iteration in range(ITERS):
        padded = with_halo(direction.astype(jnp.bfloat16), (("grid", 1),), 4).astype(
            direction.dtype
        )
        padded = jnp.pad(padded, ((0, 0), (0, 0), (4, 4), (4, 4)))
        kinetic = -0.5 * second_sum(padded, width_x, width_y, width_z)
        rounded = direction.astype(jnp.bfloat16).reshape(local_bands, local_cells)
        gathered = lax.all_to_all(
            jnp.concatenate([rounded] * band_count, axis=0), "band", 0, 0, tiled=True
        )
        partial_margin = lax.dot_general(
            occupied_rows, gathered, (((1,), (1,)), ((), ())), preferred_element_type=jnp.float32
        )
        margins = grid_sum(partial_margin, "grid")
        scaled = (margins * weight_scale).astype(jnp.bfloat16)
        terms = lax.dot_general(
            scaled, occupied_rows, (((0,), (0,)), ((), ())), preferred_element_type=jnp.float32
        ).astype(jnp.bfloat16)
        received = lax.all_to_all(terms, "band", 0, 0, tiled=True).astype(jnp.float32)
        projected = received.reshape(band_count, local_bands, local_cells).sum(axis=0)
        applied = kinetic + potential_shift * direction + projected.reshape(direction.shape)
        curvature = grid_sum(inner_product(direction, applied), "grid")
        step_size = norm_now / curvature
        solution = solution + expand(step_size) * direction
        residual = residual - expand(step_size) * applied
        if iteration + 1 < ITERS:
            norm_next = grid_sum(inner_product(residual, residual), "grid")
            direction = residual + expand(norm_next / norm_now) * direction
            norm_now = norm_next
    return (solution, residual)


def body(occupied, potential, shifts, source_term):
    pieces = 2 if source_term.shape[0] % 2 == 0 else 1
    width = source_term.shape[0] // pieces
    results = [
        chain(occupied, potential, shifts[k * width : (k + 1) * width], source_term[k * width : (k + 1) * width])
        for k in range(pieces)
    ]
    return tuple(jnp.concatenate([r[i] for r in results], axis=0) for i in range(2))


def solution(mesh):
    in_specs = (
        P("band", "grid", None, None),
        P("grid", None, None),
        P("band"),
        P("band", "grid", None, None),
    )
    out_specs = (P("band", "grid", None, None), P("band", "grid", None, None))
    return jax.shard_map(body, mesh=mesh, in_specs=in_specs, out_specs=out_specs, check_vma=False)
```

```python
import math

import jax
import jax.numpy as jnp
from jax import lax
from jax.sharding import PartitionSpec as P

ITERS = 2


COEFFICIENTS = (-205.0 / 72.0, 8.0 / 5.0, -1.0 / 5.0, 8.0 / 315.0, -1.0 / 560.0)


def with_halo(shard, sides, width):
    for axis, dim in sides:
        peers, length = (lax.axis_size(axis), shard.shape[dim])
        up = [(i, (i + 1) % peers) for i in range(peers - 1)]
        down = [(j, i) for i, j in up]
        last = lax.slice_in_dim(shard, length - width, length, axis=dim)
        leading = lax.slice_in_dim(shard, 0, width, axis=dim)
        before = lax.ppermute(last, axis, up)
        after = lax.ppermute(leading, axis, down)
        shard = jnp.concatenate([before, shard, after], axis=dim)
    return shard


def grid_sum(value, axis):
    peers = lax.axis_size(axis)
    assert peers & (peers - 1) == 0
    stride = 1
    while stride < peers:
        pairs = [(i, i ^ stride) for i in range(peers)]
        value = value + lax.ppermute(value, axis, pairs)
        stride *= 2
    return value


def second_sum(padded, extent_x, extent_y, extent_z):
    middle = padded[:, 4 : 4 + extent_x, 4 : 4 + extent_y, 4 : 4 + extent_z]
    summed = 3.0 * COEFFICIENTS[0] * middle
    for offset in range(1, 5):
        along_x = (
            padded[:, 4 + offset : 4 + offset + extent_x, 4 : 4 + extent_y, 4 : 4 + extent_z]
            + padded[:, 4 - offset : 4 - offset + extent_x, 4 : 4 + extent_y, 4 : 4 + extent_z]
        )
        along_y = (
            padded[:, 4 : 4 + extent_x, 4 + offset : 4 + offset + extent_y, 4 : 4 + extent_z]
            + padded[:, 4 : 4 + extent_x, 4 - offset : 4 - offset + extent_y, 4 : 4 + extent_z]
        )
        along_z = (
            padded[:, 4 : 4 + extent_x, 4 : 4 + extent_y, 4 + offset : 4 + offset + extent_z]
            + padded[:, 4 : 4 + extent_x, 4 : 4 + extent_y, 4 - offset : 4 - offset + extent_z]
        )
        summed = (
            summed
            + COEFFICIENTS[offset] * along_x
            + COEFFICIENTS[offset] * along_y
            + COEFFICIENTS[offset] * along_z
        )
    return summed


def inner_product(first_field, second_field):
    return jnp.sum(first_field * second_field, axis=(1, 2, 3))


def expand(vector):
    return vector[:, None, None, None]


def chain(occupied, potential, shifts, source_term):
    local_bands, width_x, width_y, width_z = source_term.shape
    local_occupied = occupied.shape[0]
    band_count = lax.axis_size("band")
    local_cells = width_x * width_y * width_z
    weight_scale = 2.0 / math.sqrt(
        local_occupied * band_count * local_cells * lax.axis_size("grid")
    )
    occupied_rows = occupied.reshape(local_occupied, local_cells)
    solution = jnp.zeros_like(source_term)
    residual = source_term
    direction = source_term
    norm_now = grid_sum(inner_product(source_term, source_term), "grid")
    for iteration in range(ITERS):
        own_potential, direction = lax.optimization_barrier((potential, direction))
        potential_shift = own_potential[None] + shifts[:, None, None, None]
        padded = with_halo(direction.astype(jnp.bfloat16), (("grid", 1),), 4).astype(
            direction.dtype
        )
        padded = jnp.pad(padded, ((0, 0), (0, 0), (4, 4), (4, 4)))
        kinetic = -0.5 * second_sum(padded, width_x, width_y, width_z)
        rounded = direction.astype(jnp.bfloat16).reshape(local_bands, local_cells)
        blocks = [rounded] + [
            lax.ppermute(rounded, "band", [(i, (i + d) % band_count) for i in range(band_count)])
            for d in range(1, band_count)
        ]
        gathered = jnp.concatenate(blocks, axis=0)
        partial_margin = lax.dot_general(
            occupied_rows, gathered, (((1,), (1,)), ((), ())), preferred_element_type=jnp.float32
        )
        margins = grid_sum(partial_margin, "grid")
        scaled = (margins * weight_scale).astype(jnp.bfloat16)
        terms = lax.dot_general(
            scaled, occupied_rows, (((0,), (0,)), ((), ())), preferred_element_type=jnp.float32
        ).astype(jnp.bfloat16)
        projected = terms[:local_bands].astype(jnp.float32)
        for d in range(1, band_count):
            part = terms[d * local_bands : (d + 1) * local_bands]
            back = lax.ppermute(part, "band", [((i + d) % band_count, i) for i in range(band_count)])
            projected = projected + back.astype(jnp.float32)
        applied = kinetic + potential_shift * direction + projected.reshape(direction.shape)
        curvature = grid_sum(inner_product(direction, applied), "grid")
        step_size = norm_now / curvature
        solution = solution + expand(step_size) * direction
        residual = residual - expand(step_size) * applied
        if iteration + 1 < ITERS:
            norm_next = grid_sum(inner_product(residual, residual), "grid")
            direction = residual + expand(norm_next / norm_now) * direction
            norm_now = norm_next
    return (solution, residual)


def body(occupied, potential, shifts, source_term):
    pieces = 2 if source_term.shape[0] % 2 == 0 else 1
    width = source_term.shape[0] // pieces
    results = [
        chain(occupied, potential, shifts[k * width : (k + 1) * width], source_term[k * width : (k + 1) * width])
        for k in range(pieces)
    ]
    return tuple(jnp.concatenate([r[i] for r in results], axis=0) for i in range(2))


def solution(mesh):
    in_specs = (
        P("band", "grid", None, None),
        P("grid", None, None),
        P("band"),
        P("band", "grid", None, None),
    )
    out_specs = (P("band", "grid", None, None), P("band", "grid", None, None))
    return jax.shard_map(body, mesh=mesh, in_specs=in_specs, out_specs=out_specs, check_vma=False)
```

```python
import math

import jax
import jax.numpy as jnp
from jax import lax
from jax.sharding import PartitionSpec as P

ITERS = 2


COEFFICIENTS = (-205.0 / 72.0, 8.0 / 5.0, -1.0 / 5.0, 8.0 / 315.0, -1.0 / 560.0)


def with_halo(shard, sides, width):
    for axis, dim in sides:
        peers, length = (lax.axis_size(axis), shard.shape[dim])
        up = [(i, (i + 1) % peers) for i in range(peers - 1)]
        down = [(j, i) for i, j in up]
        last = lax.slice_in_dim(shard, length - width, length, axis=dim)
        leading = lax.slice_in_dim(shard, 0, width, axis=dim)
        before = lax.ppermute(last, axis, up)
        after = lax.ppermute(leading, axis, down)
        shard = jnp.concatenate([before, shard, after], axis=dim)
    return shard


def grid_sum(value, axis):
    peers = lax.axis_size(axis)
    assert peers & (peers - 1) == 0
    stride = 1
    while stride < peers:
        pairs = [(i, i ^ stride) for i in range(peers)]
        value = value + lax.ppermute(value, axis, pairs)
        stride *= 2
    return value


def second_sum(padded, extent_x, extent_y, extent_z):
    middle = padded[:, 4 : 4 + extent_x, 4 : 4 + extent_y, 4 : 4 + extent_z]
    summed = 3.0 * COEFFICIENTS[0] * middle
    for offset in range(1, 5):
        along_x = (
            padded[:, 4 + offset : 4 + offset + extent_x, 4 : 4 + extent_y, 4 : 4 + extent_z]
            + padded[:, 4 - offset : 4 - offset + extent_x, 4 : 4 + extent_y, 4 : 4 + extent_z]
        )
        along_y = (
            padded[:, 4 : 4 + extent_x, 4 + offset : 4 + offset + extent_y, 4 : 4 + extent_z]
            + padded[:, 4 : 4 + extent_x, 4 - offset : 4 - offset + extent_y, 4 : 4 + extent_z]
        )
        along_z = (
            padded[:, 4 : 4 + extent_x, 4 : 4 + extent_y, 4 + offset : 4 + offset + extent_z]
            + padded[:, 4 : 4 + extent_x, 4 : 4 + extent_y, 4 - offset : 4 - offset + extent_z]
        )
        summed = (
            summed
            + COEFFICIENTS[offset] * along_x
            + COEFFICIENTS[offset] * along_y
            + COEFFICIENTS[offset] * along_z
        )
    return summed


def inner_product(first_field, second_field):
    return jnp.sum(first_field * second_field, axis=(1, 2, 3))


def expand(vector):
    return vector[:, None, None, None]


def chain(occupied, potential, shifts, source_term):
    local_bands, width_x, width_y, width_z = source_term.shape
    local_occupied = occupied.shape[0]
    band_count = lax.axis_size("band")
    local_cells = width_x * width_y * width_z
    weight_scale = 2.0 / math.sqrt(
        local_occupied * band_count * local_cells * lax.axis_size("grid")
    )
    occupied_rows = occupied.reshape(local_occupied, local_cells)
    solution = jnp.zeros_like(source_term)
    residual = source_term
    direction = source_term
    norm_now = grid_sum(inner_product(source_term, source_term), "grid")
    shift_pairs = [[(i, (i + d) % band_count) for i in range(band_count)] for d in range(1, band_count)]
    previous_margins = None
    for iteration in range(ITERS):
        own_potential, direction = lax.optimization_barrier((potential, direction))
        potential_shift = own_potential[None] + shifts[:, None, None, None]
        padded = with_halo(direction.astype(jnp.bfloat16), (("grid", 1),), 4).astype(
            direction.dtype
        )
        padded = jnp.pad(padded, ((0, 0), (0, 0), (4, 4), (4, 4)))
        kinetic = -0.5 * second_sum(padded, width_x, width_y, width_z)
        fresh = direction if previous_margins is None else residual
        rounded = fresh.astype(jnp.bfloat16).reshape(local_bands, local_cells)
        blocks = [rounded] + [lax.ppermute(rounded, "band", pairs) for pairs in shift_pairs]
        gathered = jnp.concatenate(blocks, axis=0)
        partial_margin = lax.dot_general(
            occupied_rows, gathered, (((1,), (1,)), ((), ())), preferred_element_type=jnp.float32
        )
        margins = grid_sum(partial_margin, "grid")
        if previous_margins is not None:
            margins = margins + beta_all[None, :] * previous_margins
        previous_margins = margins
        scaled = (margins * weight_scale).astype(jnp.bfloat16)
        terms = lax.dot_general(
            scaled, occupied_rows, (((0,), (0,)), ((), ())), preferred_element_type=jnp.float32
        ).astype(jnp.bfloat16)
        projected = terms[:local_bands].astype(jnp.float32)
        for d in range(1, band_count):
            part = terms[d * local_bands : (d + 1) * local_bands]
            back = lax.ppermute(part, "band", [((i + d) % band_count, i) for i in range(band_count)])
            projected = projected + back.astype(jnp.float32)
        applied = kinetic + potential_shift * direction + projected.reshape(direction.shape)
        curvature = grid_sum(inner_product(direction, applied), "grid")
        step_size = norm_now / curvature
        solution = solution + expand(step_size) * direction
        residual = residual - expand(step_size) * applied
        if iteration + 1 < ITERS:
            norm_next = grid_sum(inner_product(residual, residual), "grid")
            beta = norm_next / norm_now
            beta_all = jnp.concatenate([beta] + [lax.ppermute(beta, "band", pairs) for pairs in shift_pairs])
            direction = residual + expand(beta) * direction
            norm_now = norm_next
    return (solution, residual)


def body(occupied, potential, shifts, source_term):
    pieces = 2 if source_term.shape[0] % 2 == 0 else 1
    width = source_term.shape[0] // pieces
    results = [
        chain(occupied, potential, shifts[k * width : (k + 1) * width], source_term[k * width : (k + 1) * width])
        for k in range(pieces)
    ]
    return tuple(jnp.concatenate([r[i] for r in results], axis=0) for i in range(2))


def solution(mesh):
    in_specs = (
        P("band", "grid", None, None),
        P("grid", None, None),
        P("band"),
        P("band", "grid", None, None),
    )
    out_specs = (P("band", "grid", None, None), P("band", "grid", None, None))
    return jax.shard_map(body, mesh=mesh, in_specs=in_specs, out_specs=out_specs, check_vma=False)
```

```python
import math

import jax
import jax.numpy as jnp
from jax import lax
from jax.sharding import PartitionSpec as P

ITERS = 2


COEFFICIENTS = (-205.0 / 72.0, 8.0 / 5.0, -1.0 / 5.0, 8.0 / 315.0, -1.0 / 560.0)


def with_halo(shard, sides, width):
    for axis, dim in sides:
        peers, length = (lax.axis_size(axis), shard.shape[dim])
        up = [(i, (i + 1) % peers) for i in range(peers - 1)]
        down = [(j, i) for i, j in up]
        last = lax.slice_in_dim(shard, length - width, length, axis=dim)
        leading = lax.slice_in_dim(shard, 0, width, axis=dim)
        before = lax.ppermute(last, axis, up)
        after = lax.ppermute(leading, axis, down)
        shard = jnp.concatenate([before, shard, after], axis=dim)
    return shard


def grid_sum(value, axis):
    peers = lax.axis_size(axis)
    assert peers & (peers - 1) == 0
    stride = 1
    while stride < peers:
        pairs = [(i, i ^ stride) for i in range(peers)]
        value = value + lax.ppermute(value, axis, pairs)
        stride *= 2
    return value


def second_sum(padded, extent_x, extent_y, extent_z):
    middle = padded[:, 4 : 4 + extent_x, 4 : 4 + extent_y, 4 : 4 + extent_z]
    summed = 3.0 * COEFFICIENTS[0] * middle
    for offset in range(1, 5):
        along_x = (
            padded[:, 4 + offset : 4 + offset + extent_x, 4 : 4 + extent_y, 4 : 4 + extent_z]
            + padded[:, 4 - offset : 4 - offset + extent_x, 4 : 4 + extent_y, 4 : 4 + extent_z]
        )
        along_y = (
            padded[:, 4 : 4 + extent_x, 4 + offset : 4 + offset + extent_y, 4 : 4 + extent_z]
            + padded[:, 4 : 4 + extent_x, 4 - offset : 4 - offset + extent_y, 4 : 4 + extent_z]
        )
        along_z = (
            padded[:, 4 : 4 + extent_x, 4 : 4 + extent_y, 4 + offset : 4 + offset + extent_z]
            + padded[:, 4 : 4 + extent_x, 4 : 4 + extent_y, 4 - offset : 4 - offset + extent_z]
        )
        summed = (
            summed
            + COEFFICIENTS[offset] * along_x
            + COEFFICIENTS[offset] * along_y
            + COEFFICIENTS[offset] * along_z
        )
    return summed


def inner_product(first_field, second_field):
    return jnp.sum(first_field * second_field, axis=(1, 2, 3))


def expand(vector):
    return vector[:, None, None, None]


def chain(occupied, potential, shifts, source_term, after):
    local_bands, width_x, width_y, width_z = source_term.shape
    local_occupied = occupied.shape[0]
    band_count = lax.axis_size("band")
    local_cells = width_x * width_y * width_z
    weight_scale = 2.0 / math.sqrt(
        local_occupied * band_count * local_cells * lax.axis_size("grid")
    )
    occupied_rows = occupied.reshape(local_occupied, local_cells)
    solution = jnp.zeros_like(source_term)
    residual = source_term
    direction = source_term
    norm_now = grid_sum(inner_product(source_term, source_term), "grid")
    arrivals = []
    for iteration in range(ITERS):
        own_potential, direction = lax.optimization_barrier((potential, direction))
        potential_shift = own_potential[None] + shifts[:, None, None, None]
        padded = with_halo(direction.astype(jnp.bfloat16), (("grid", 1),), 4).astype(
            direction.dtype
        )
        padded = jnp.pad(padded, ((0, 0), (0, 0), (4, 4), (4, 4)))
        kinetic = -0.5 * second_sum(padded, width_x, width_y, width_z)
        if after is not None:
            direction, _ = lax.optimization_barrier((direction, after[iteration]))
        rounded = direction.astype(jnp.bfloat16).reshape(local_bands, local_cells)
        blocks = [rounded] + [
            lax.ppermute(rounded, "band", [(i, (i + d) % band_count) for i in range(band_count)])
            for d in range(1, band_count)
        ]
        gathered = jnp.concatenate(blocks, axis=0)
        arrivals.append(gathered)
        partial_margin = lax.dot_general(
            occupied_rows, gathered, (((1,), (1,)), ((), ())), preferred_element_type=jnp.float32
        )
        margins = grid_sum(partial_margin, "grid")
        scaled = (margins * weight_scale).astype(jnp.bfloat16)
        terms = lax.dot_general(
            scaled, occupied_rows, (((0,), (0,)), ((), ())), preferred_element_type=jnp.float32
        ).astype(jnp.bfloat16)
        projected = terms[:local_bands].astype(jnp.float32)
        for d in range(1, band_count):
            part = terms[d * local_bands : (d + 1) * local_bands]
            back = lax.ppermute(part, "band", [((i + d) % band_count, i) for i in range(band_count)])
            projected = projected + back.astype(jnp.float32)
        applied = kinetic + potential_shift * direction + projected.reshape(direction.shape)
        curvature = grid_sum(inner_product(direction, applied), "grid")
        step_size = norm_now / curvature
        solution = solution + expand(step_size) * direction
        residual = residual - expand(step_size) * applied
        if iteration + 1 < ITERS:
            norm_next = grid_sum(inner_product(residual, residual), "grid")
            direction = residual + expand(norm_next / norm_now) * direction
            norm_now = norm_next
    return (solution, residual, arrivals)


def body(occupied, potential, shifts, source_term):
    pieces = 2 if source_term.shape[0] % 2 == 0 else 1
    width = source_term.shape[0] // pieces
    results = []
    after = None
    for k in range(pieces):
        result = chain(
            occupied,
            potential,
            shifts[k * width : (k + 1) * width],
            source_term[k * width : (k + 1) * width],
            after,
        )
        after = result[2]
        results.append(result)
    return tuple(jnp.concatenate([r[i] for r in results], axis=0) for i in range(2))


def solution(mesh):
    in_specs = (
        P("band", "grid", None, None),
        P("grid", None, None),
        P("band"),
        P("band", "grid", None, None),
    )
    out_specs = (P("band", "grid", None, None), P("band", "grid", None, None))
    return jax.shard_map(body, mesh=mesh, in_specs=in_specs, out_specs=out_specs, check_vma=False)
```

```python
import math

import jax
import jax.numpy as jnp
from jax import lax
from jax.sharding import PartitionSpec as P

ITERS = 2


COEFFICIENTS = (-205.0 / 72.0, 8.0 / 5.0, -1.0 / 5.0, 8.0 / 315.0, -1.0 / 560.0)


def with_halo(shard, sides, width):
    for axis, dim in sides:
        peers, length = (lax.axis_size(axis), shard.shape[dim])
        up = [(i, (i + 1) % peers) for i in range(peers - 1)]
        down = [(j, i) for i, j in up]
        last = lax.slice_in_dim(shard, length - width, length, axis=dim)
        leading = lax.slice_in_dim(shard, 0, width, axis=dim)
        before = lax.ppermute(last, axis, up)
        after = lax.ppermute(leading, axis, down)
        shard = jnp.concatenate([before, shard, after], axis=dim)
    return shard


def grid_sum(value, axis):
    peers = lax.axis_size(axis)
    assert peers & (peers - 1) == 0
    stride = 1
    while stride < peers:
        pairs = [(i, i ^ stride) for i in range(peers)]
        value = value + lax.ppermute(value, axis, pairs)
        stride *= 2
    return value


def second_sum(padded, extent_x, extent_y, extent_z):
    middle = padded[:, 4 : 4 + extent_x, 4 : 4 + extent_y, 4 : 4 + extent_z]
    summed = 3.0 * COEFFICIENTS[0] * middle
    for offset in range(1, 5):
        along_x = (
            padded[:, 4 + offset : 4 + offset + extent_x, 4 : 4 + extent_y, 4 : 4 + extent_z]
            + padded[:, 4 - offset : 4 - offset + extent_x, 4 : 4 + extent_y, 4 : 4 + extent_z]
        )
        along_y = (
            padded[:, 4 : 4 + extent_x, 4 + offset : 4 + offset + extent_y, 4 : 4 + extent_z]
            + padded[:, 4 : 4 + extent_x, 4 - offset : 4 - offset + extent_y, 4 : 4 + extent_z]
        )
        along_z = (
            padded[:, 4 : 4 + extent_x, 4 : 4 + extent_y, 4 + offset : 4 + offset + extent_z]
            + padded[:, 4 : 4 + extent_x, 4 : 4 + extent_y, 4 - offset : 4 - offset + extent_z]
        )
        summed = (
            summed
            + COEFFICIENTS[offset] * along_x
            + COEFFICIENTS[offset] * along_y
            + COEFFICIENTS[offset] * along_z
        )
    return summed


def inner_product(first_field, second_field):
    return jnp.sum(first_field * second_field, axis=(1, 2, 3))


def expand(vector):
    return vector[:, None, None, None]


def body(occupied, potential, shifts, source_term):
    local_bands, width_x, width_y, width_z = source_term.shape
    local_occupied = occupied.shape[0]
    band_count = lax.axis_size("band")
    local_cells = width_x * width_y * width_z
    weight_scale = 2.0 / math.sqrt(
        local_occupied * band_count * local_cells * lax.axis_size("grid")
    )
    occupied_rows = occupied.reshape(local_occupied, local_cells)
    potential_shift = potential[None] + shifts[:, None, None, None]
    solution = jnp.zeros_like(source_term)
    residual = source_term
    direction = source_term
    norm_now = grid_sum(inner_product(source_term, source_term), "grid")
    for iteration in range(ITERS):
        padded = with_halo(direction.astype(jnp.bfloat16), (("grid", 1),), 4).astype(
            direction.dtype
        )
        padded = jnp.pad(padded, ((0, 0), (0, 0), (4, 4), (4, 4)))
        kinetic = -0.5 * second_sum(padded, width_x, width_y, width_z)
        rounded = direction.astype(jnp.bfloat16).reshape(local_bands, local_cells)
        halves = 2 if local_bands % 2 == 0 else 1
        half = local_bands // halves
        partial_margin = jnp.concatenate(
            [
                lax.dot_general(
                    occupied_rows,
                    jnp.concatenate(
                        [rounded[h * half : (h + 1) * half]]
                        + [
                            lax.ppermute(
                                rounded[h * half : (h + 1) * half],
                                "band",
                                [(i, (i + d) % band_count) for i in range(band_count)],
                            )
                            for d in range(1, band_count)
                        ],
                        axis=0,
                    ),
                    (((1,), (1,)), ((), ())),
                    preferred_element_type=jnp.float32,
                )
                for h in range(halves)
            ],
            axis=1,
        )
        margins = grid_sum(partial_margin, "grid")
        scaled = (margins * weight_scale).astype(jnp.bfloat16)
        pieces = []
        for h in range(halves):
            terms = lax.dot_general(
                scaled[:, h * band_count * half : (h + 1) * band_count * half],
                occupied_rows,
                (((0,), (0,)), ((), ())),
                preferred_element_type=jnp.float32,
            ).astype(jnp.bfloat16)
            piece = terms[:half].astype(jnp.float32)
            for d in range(1, band_count):
                part = terms[d * half : (d + 1) * half]
                back = lax.ppermute(part, "band", [((i + d) % band_count, i) for i in range(band_count)])
                piece = piece + back.astype(jnp.float32)
            pieces.append(piece)
        projected = jnp.concatenate(pieces, axis=0)
        applied = kinetic + potential_shift * direction + projected.reshape(direction.shape)
        curvature = grid_sum(inner_product(direction, applied), "grid")
        step_size = norm_now / curvature
        solution = solution + expand(step_size) * direction
        residual = residual - expand(step_size) * applied
        if iteration + 1 < ITERS:
            norm_next = grid_sum(inner_product(residual, residual), "grid")
            direction = residual + expand(norm_next / norm_now) * direction
            norm_now = norm_next
    return (solution, residual)


def solution(mesh):
    in_specs = (
        P("band", "grid", None, None),
        P("grid", None, None),
        P("band"),
        P("band", "grid", None, None),
    )
    out_specs = (P("band", "grid", None, None), P("band", "grid", None, None))
    return jax.shard_map(body, mesh=mesh, in_specs=in_specs, out_specs=out_specs, check_vma=False)
```

```python
import math

import jax
import jax.numpy as jnp
from jax import lax
from jax.sharding import PartitionSpec as P

ITERS = 2


COEFFICIENTS = (-205.0 / 72.0, 8.0 / 5.0, -1.0 / 5.0, 8.0 / 315.0, -1.0 / 560.0)


def with_halo(shard, sides, width):
    for axis, dim in sides:
        peers, length = (lax.axis_size(axis), shard.shape[dim])
        up = [(i, (i + 1) % peers) for i in range(peers - 1)]
        down = [(j, i) for i, j in up]
        last = lax.slice_in_dim(shard, length - width, length, axis=dim)
        leading = lax.slice_in_dim(shard, 0, width, axis=dim)
        before = lax.ppermute(last, axis, up)
        after = lax.ppermute(leading, axis, down)
        shard = jnp.concatenate([before, shard, after], axis=dim)
    return shard


def grid_sum(value, axis):
    peers = lax.axis_size(axis)
    assert peers & (peers - 1) == 0
    stride = 1
    while stride < peers:
        pairs = [(i, i ^ stride) for i in range(peers)]
        value = value + lax.ppermute(value, axis, pairs)
        stride *= 2
    return value


def second_sum(padded, extent_x, extent_y, extent_z):
    middle = padded[:, 4 : 4 + extent_x, 4 : 4 + extent_y, 4 : 4 + extent_z]
    summed = 3.0 * COEFFICIENTS[0] * middle
    for offset in range(1, 5):
        along_x = (
            padded[:, 4 + offset : 4 + offset + extent_x, 4 : 4 + extent_y, 4 : 4 + extent_z]
            + padded[:, 4 - offset : 4 - offset + extent_x, 4 : 4 + extent_y, 4 : 4 + extent_z]
        )
        along_y = (
            padded[:, 4 : 4 + extent_x, 4 + offset : 4 + offset + extent_y, 4 : 4 + extent_z]
            + padded[:, 4 : 4 + extent_x, 4 - offset : 4 - offset + extent_y, 4 : 4 + extent_z]
        )
        along_z = (
            padded[:, 4 : 4 + extent_x, 4 : 4 + extent_y, 4 + offset : 4 + offset + extent_z]
            + padded[:, 4 : 4 + extent_x, 4 : 4 + extent_y, 4 - offset : 4 - offset + extent_z]
        )
        summed = (
            summed
            + COEFFICIENTS[offset] * along_x
            + COEFFICIENTS[offset] * along_y
            + COEFFICIENTS[offset] * along_z
        )
    return summed


def inner_product(first_field, second_field):
    return jnp.sum(first_field * second_field, axis=(1, 2, 3))


def expand(vector):
    return vector[:, None, None, None]


def body(occupied, potential, shifts, source_term):
    total_bands, width_x, width_y, width_z = source_term.shape
    local_occupied = occupied.shape[0]
    band_count = lax.axis_size("band")
    local_cells = width_x * width_y * width_z
    weight_scale = 2.0 / math.sqrt(
        local_occupied * band_count * local_cells * lax.axis_size("grid")
    )
    occupied_rows = occupied.reshape(local_occupied, local_cells)
    pieces = 2 if total_bands % 2 == 0 else 1
    local_bands = total_bands // pieces
    spans = [slice(k * local_bands, (k + 1) * local_bands) for k in range(pieces)]
    norm_all = grid_sum(inner_product(source_term, source_term), "grid")
    solution = [jnp.zeros_like(source_term[span]) for span in spans]
    residual = [source_term[span] for span in spans]
    direction = [source_term[span] for span in spans]
    norm_now = [norm_all[span] for span in spans]
    for iteration in range(ITERS):
        whole = jnp.concatenate(direction, axis=0) if pieces > 1 else direction[0]
        padded = with_halo(whole.astype(jnp.bfloat16), (("grid", 1),), 4).astype(whole.dtype)
        padded = jnp.pad(padded, ((0, 0), (0, 0), (4, 4), (4, 4)))
        kinetic_all = -0.5 * second_sum(padded, width_x, width_y, width_z)
        for k, span in enumerate(spans):
            own_potential, current = lax.optimization_barrier((potential, direction[k]))
            potential_shift = own_potential[None] + shifts[span][:, None, None, None]
            rounded = current.astype(jnp.bfloat16).reshape(local_bands, local_cells)
            blocks = [rounded] + [
                lax.ppermute(rounded, "band", [(i, (i + d) % band_count) for i in range(band_count)])
                for d in range(1, band_count)
            ]
            gathered = jnp.concatenate(blocks, axis=0)
            partial_margin = lax.dot_general(
                occupied_rows, gathered, (((1,), (1,)), ((), ())), preferred_element_type=jnp.float32
            )
            margins = grid_sum(partial_margin, "grid")
            scaled = (margins * weight_scale).astype(jnp.bfloat16)
            terms = lax.dot_general(
                scaled, occupied_rows, (((0,), (0,)), ((), ())), preferred_element_type=jnp.float32
            ).astype(jnp.bfloat16)
            projected = terms[:local_bands].astype(jnp.float32)
            for d in range(1, band_count):
                part = terms[d * local_bands : (d + 1) * local_bands]
                back = lax.ppermute(part, "band", [((i + d) % band_count, i) for i in range(band_count)])
                projected = projected + back.astype(jnp.float32)
            applied = kinetic_all[span] + potential_shift * current + projected.reshape(current.shape)
            curvature = grid_sum(inner_product(current, applied), "grid")
            step_size = norm_now[k] / curvature
            solution[k] = solution[k] + expand(step_size) * current
            residual[k] = residual[k] - expand(step_size) * applied
            if iteration + 1 < ITERS:
                norm_next = grid_sum(inner_product(residual[k], residual[k]), "grid")
                direction[k] = residual[k] + expand(norm_next / norm_now[k]) * current
                norm_now[k] = norm_next
    return (jnp.concatenate(solution, axis=0), jnp.concatenate(residual, axis=0))


def solution(mesh):
    in_specs = (
        P("band", "grid", None, None),
        P("grid", None, None),
        P("band"),
        P("band", "grid", None, None),
    )
    out_specs = (P("band", "grid", None, None), P("band", "grid", None, None))
    return jax.shard_map(body, mesh=mesh, in_specs=in_specs, out_specs=out_specs, check_vma=False)
```

```python
import math

import jax
import jax.numpy as jnp
from jax import lax
from jax.sharding import PartitionSpec as P

ITERS = 2


COEFFICIENTS = (-205.0 / 72.0, 8.0 / 5.0, -1.0 / 5.0, 8.0 / 315.0, -1.0 / 560.0)


def with_halo(shard, sides, width):
    for axis, dim in sides:
        peers, length = (lax.axis_size(axis), shard.shape[dim])
        up = [(i, (i + 1) % peers) for i in range(peers - 1)]
        down = [(j, i) for i, j in up]
        last = lax.slice_in_dim(shard, length - width, length, axis=dim)
        leading = lax.slice_in_dim(shard, 0, width, axis=dim)
        before = lax.ppermute(last, axis, up)
        after = lax.ppermute(leading, axis, down)
        shard = jnp.concatenate([before, shard, after], axis=dim)
    return shard


def grid_sum(value, axis):
    peers = lax.axis_size(axis)
    assert peers & (peers - 1) == 0
    stride = 1
    while stride < peers:
        pairs = [(i, i ^ stride) for i in range(peers)]
        value = value + lax.ppermute(value, axis, pairs)
        stride *= 2
    return value


def second_sum(padded, extent_x, extent_y, extent_z):
    middle = padded[:, 4 : 4 + extent_x, 4 : 4 + extent_y, 4 : 4 + extent_z]
    summed = 3.0 * COEFFICIENTS[0] * middle
    for offset in range(1, 5):
        along_x = (
            padded[:, 4 + offset : 4 + offset + extent_x, 4 : 4 + extent_y, 4 : 4 + extent_z]
            + padded[:, 4 - offset : 4 - offset + extent_x, 4 : 4 + extent_y, 4 : 4 + extent_z]
        )
        along_y = (
            padded[:, 4 : 4 + extent_x, 4 + offset : 4 + offset + extent_y, 4 : 4 + extent_z]
            + padded[:, 4 : 4 + extent_x, 4 - offset : 4 - offset + extent_y, 4 : 4 + extent_z]
        )
        along_z = (
            padded[:, 4 : 4 + extent_x, 4 : 4 + extent_y, 4 + offset : 4 + offset + extent_z]
            + padded[:, 4 : 4 + extent_x, 4 : 4 + extent_y, 4 - offset : 4 - offset + extent_z]
        )
        summed = (
            summed
            + COEFFICIENTS[offset] * along_x
            + COEFFICIENTS[offset] * along_y
            + COEFFICIENTS[offset] * along_z
        )
    return summed


def inner_product(first_field, second_field):
    return jnp.sum(first_field * second_field, axis=(1, 2, 3))


def expand(vector):
    return vector[:, None, None, None]


def chain(occupied, potential, shifts, source_term):
    local_bands, width_x, width_y, width_z = source_term.shape
    local_occupied = occupied.shape[0]
    band_count = lax.axis_size("band")
    local_cells = width_x * width_y * width_z
    weight_scale = 2.0 / math.sqrt(
        local_occupied * band_count * local_cells * lax.axis_size("grid")
    )
    occupied_rows = occupied.reshape(local_occupied, local_cells)
    solution = jnp.zeros_like(source_term)
    residual = source_term
    direction = source_term
    norm_now = grid_sum(inner_product(source_term, source_term), "grid")
    for iteration in range(ITERS):
        own_potential, direction = lax.optimization_barrier((potential, direction))
        potential_shift = own_potential[None] + shifts[:, None, None, None]
        padded = with_halo(direction.astype(jnp.bfloat16), (("grid", 1),), 4).astype(
            direction.dtype
        )
        padded = jnp.pad(padded, ((0, 0), (0, 0), (4, 4), (4, 4)))
        kinetic = -0.5 * second_sum(padded, width_x, width_y, width_z)
        rounded = direction.astype(jnp.bfloat16).reshape(local_bands, local_cells)
        order = sorted(range(1, band_count), key=lambda d: (min(d, band_count - d), -d))
        arrived = {
            d: lax.ppermute(rounded, "band", [(i, (i + d) % band_count) for i in range(band_count)])
            for d in order
        }
        blocks = [rounded] + [arrived[d] for d in range(1, band_count)]
        gathered = jnp.concatenate(blocks, axis=0)
        partial_margin = lax.dot_general(
            occupied_rows, gathered, (((1,), (1,)), ((), ())), preferred_element_type=jnp.float32
        )
        margins = grid_sum(partial_margin, "grid")
        scaled = (margins * weight_scale).astype(jnp.bfloat16)
        terms = lax.dot_general(
            scaled, occupied_rows, (((0,), (0,)), ((), ())), preferred_element_type=jnp.float32
        ).astype(jnp.bfloat16)
        projected = terms[:local_bands].astype(jnp.float32)
        for d in order:
            part = terms[d * local_bands : (d + 1) * local_bands]
            back = lax.ppermute(part, "band", [((i + d) % band_count, i) for i in range(band_count)])
            projected = projected + back.astype(jnp.float32)
        applied = kinetic + potential_shift * direction + projected.reshape(direction.shape)
        curvature = grid_sum(inner_product(direction, applied), "grid")
        step_size = norm_now / curvature
        solution = solution + expand(step_size) * direction
        residual = residual - expand(step_size) * applied
        if iteration + 1 < ITERS:
            norm_next = grid_sum(inner_product(residual, residual), "grid")
            direction = residual + expand(norm_next / norm_now) * direction
            norm_now = norm_next
    return (solution, residual)


def body(occupied, potential, shifts, source_term):
    pieces = 2 if source_term.shape[0] % 2 == 0 else 1
    width = source_term.shape[0] // pieces
    results = [
        chain(occupied, potential, shifts[k * width : (k + 1) * width], source_term[k * width : (k + 1) * width])
        for k in range(pieces)
    ]
    return tuple(jnp.concatenate([r[i] for r in results], axis=0) for i in range(2))


def solution(mesh):
    in_specs = (
        P("band", "grid", None, None),
        P("grid", None, None),
        P("band"),
        P("band", "grid", None, None),
    )
    out_specs = (P("band", "grid", None, None), P("band", "grid", None, None))
    return jax.shard_map(body, mesh=mesh, in_specs=in_specs, out_specs=out_specs, check_vma=False)
```

```python
import math

import jax
import jax.numpy as jnp
from jax import lax
from jax.sharding import PartitionSpec as P

ITERS = 2


COEFFICIENTS = (-205.0 / 72.0, 8.0 / 5.0, -1.0 / 5.0, 8.0 / 315.0, -1.0 / 560.0)


def with_halo(shard, sides, width):
    for axis, dim in sides:
        peers, length = (lax.axis_size(axis), shard.shape[dim])
        up = [(i, (i + 1) % peers) for i in range(peers - 1)]
        down = [(j, i) for i, j in up]
        last = lax.slice_in_dim(shard, length - width, length, axis=dim)
        leading = lax.slice_in_dim(shard, 0, width, axis=dim)
        before = lax.ppermute(last, axis, up)
        after = lax.ppermute(leading, axis, down)
        shard = jnp.concatenate([before, shard, after], axis=dim)
    return shard


def grid_sum(value, axis):
    peers = lax.axis_size(axis)
    assert peers & (peers - 1) == 0
    stride = 1
    while stride < peers:
        pairs = [(i, i ^ stride) for i in range(peers)]
        value = value + lax.ppermute(value, axis, pairs)
        stride *= 2
    return value


def second_sum(padded, extent_x, extent_y, extent_z):
    middle = padded[:, 4 : 4 + extent_x, 4 : 4 + extent_y, 4 : 4 + extent_z]
    summed = 3.0 * COEFFICIENTS[0] * middle
    for offset in range(1, 5):
        along_x = (
            padded[:, 4 + offset : 4 + offset + extent_x, 4 : 4 + extent_y, 4 : 4 + extent_z]
            + padded[:, 4 - offset : 4 - offset + extent_x, 4 : 4 + extent_y, 4 : 4 + extent_z]
        )
        along_y = (
            padded[:, 4 : 4 + extent_x, 4 + offset : 4 + offset + extent_y, 4 : 4 + extent_z]
            + padded[:, 4 : 4 + extent_x, 4 - offset : 4 - offset + extent_y, 4 : 4 + extent_z]
        )
        along_z = (
            padded[:, 4 : 4 + extent_x, 4 : 4 + extent_y, 4 + offset : 4 + offset + extent_z]
            + padded[:, 4 : 4 + extent_x, 4 : 4 + extent_y, 4 - offset : 4 - offset + extent_z]
        )
        summed = (
            summed
            + COEFFICIENTS[offset] * along_x
            + COEFFICIENTS[offset] * along_y
            + COEFFICIENTS[offset] * along_z
        )
    return summed


def inner_product(first_field, second_field):
    return jnp.sum(first_field * second_field, axis=(1, 2, 3))


def expand(vector):
    return vector[:, None, None, None]


def chain(occupied, potential, shifts, source_term, flip=False):
    local_bands, width_x, width_y, width_z = source_term.shape
    local_occupied = occupied.shape[0]
    band_count = lax.axis_size("band")
    local_cells = width_x * width_y * width_z
    weight_scale = 2.0 / math.sqrt(
        local_occupied * band_count * local_cells * lax.axis_size("grid")
    )
    occupied_rows = occupied.reshape(local_occupied, local_cells)
    solution = jnp.zeros_like(source_term)
    residual = source_term
    direction = source_term
    norm_now = grid_sum(inner_product(source_term, source_term), "grid")
    for iteration in range(ITERS):
        own_potential, direction = lax.optimization_barrier((potential, direction))
        potential_shift = own_potential[None] + shifts[:, None, None, None]
        padded = with_halo(direction.astype(jnp.bfloat16), (("grid", 1),), 4).astype(
            direction.dtype
        )
        padded = jnp.pad(padded, ((0, 0), (0, 0), (4, 4), (4, 4)))
        kinetic = -0.5 * second_sum(padded, width_x, width_y, width_z)
        rounded = direction.astype(jnp.bfloat16).reshape(local_bands, local_cells)
        order = sorted(range(1, band_count), key=lambda d: (min(d, band_count - d), d if flip else -d))
        arrived = {
            d: lax.ppermute(rounded, "band", [(i, (i + d) % band_count) for i in range(band_count)])
            for d in order
        }
        blocks = [rounded] + [arrived[d] for d in range(1, band_count)]
        gathered = jnp.concatenate(blocks, axis=0)
        partial_margin = lax.dot_general(
            occupied_rows, gathered, (((1,), (1,)), ((), ())), preferred_element_type=jnp.float32
        )
        margins = grid_sum(partial_margin, "grid")
        scaled = (margins * weight_scale).astype(jnp.bfloat16)
        terms = lax.dot_general(
            scaled, occupied_rows, (((0,), (0,)), ((), ())), preferred_element_type=jnp.float32
        ).astype(jnp.bfloat16)
        projected = terms[:local_bands].astype(jnp.float32)
        for d in order:
            part = terms[d * local_bands : (d + 1) * local_bands]
            back = lax.ppermute(part, "band", [((i + d) % band_count, i) for i in range(band_count)])
            projected = projected + back.astype(jnp.float32)
        applied = kinetic + potential_shift * direction + projected.reshape(direction.shape)
        curvature = grid_sum(inner_product(direction, applied), "grid")
        step_size = norm_now / curvature
        if iteration + 1 == ITERS:
            return (solution, residual, direction, applied, step_size)
        solution = solution + expand(step_size) * direction
        residual = residual - expand(step_size) * applied
        if iteration + 1 < ITERS:
            norm_next = grid_sum(inner_product(residual, residual), "grid")
            direction = residual + expand(norm_next / norm_now) * direction
            norm_now = norm_next
    return (solution, residual)


def body(occupied, potential, shifts, source_term):
    pieces = 2 if source_term.shape[0] % 2 == 0 else 1
    width = source_term.shape[0] // pieces
    results = [
        chain(
            occupied,
            potential,
            shifts[k * width : (k + 1) * width],
            source_term[k * width : (k + 1) * width],
            k % 2 == 1,
        )
        for k in range(pieces)
    ]
    solution, residual, direction, applied, step_size = (
        jnp.concatenate([r[i] for r in results], axis=0) for i in range(5)
    )
    return (solution + expand(step_size) * direction, residual - expand(step_size) * applied)


def solution(mesh):
    in_specs = (
        P("band", "grid", None, None),
        P("grid", None, None),
        P("band"),
        P("band", "grid", None, None),
    )
    out_specs = (P("band", "grid", None, None), P("band", "grid", None, None))
    return jax.shard_map(body, mesh=mesh, in_specs=in_specs, out_specs=out_specs, check_vma=False)
```

```python
import math

import jax
import jax.numpy as jnp
from jax import lax
from jax.sharding import PartitionSpec as P

ITERS = 2


COEFFICIENTS = (-205.0 / 72.0, 8.0 / 5.0, -1.0 / 5.0, 8.0 / 315.0, -1.0 / 560.0)


def with_halo(shard, sides, width):
    for axis, dim in sides:
        peers, length = (lax.axis_size(axis), shard.shape[dim])
        up = [(i, (i + 1) % peers) for i in range(peers - 1)]
        down = [(j, i) for i, j in up]
        last = lax.slice_in_dim(shard, length - width, length, axis=dim)
        leading = lax.slice_in_dim(shard, 0, width, axis=dim)
        before = lax.ppermute(last, axis, up)
        after = lax.ppermute(leading, axis, down)
        shard = jnp.concatenate([before, shard, after], axis=dim)
    return shard


def grid_sum(value, axis):
    peers = lax.axis_size(axis)
    assert peers & (peers - 1) == 0
    stride = 1
    while stride < peers:
        pairs = [(i, i ^ stride) for i in range(peers)]
        value = value + lax.ppermute(value, axis, pairs)
        stride *= 2
    return value


def second_sum(padded, extent_x, extent_y, extent_z):
    middle = padded[:, 4 : 4 + extent_x, 4 : 4 + extent_y, 4 : 4 + extent_z]
    summed = 3.0 * COEFFICIENTS[0] * middle
    for offset in range(1, 5):
        along_x = (
            padded[:, 4 + offset : 4 + offset + extent_x, 4 : 4 + extent_y, 4 : 4 + extent_z]
            + padded[:, 4 - offset : 4 - offset + extent_x, 4 : 4 + extent_y, 4 : 4 + extent_z]
        )
        along_y = (
            padded[:, 4 : 4 + extent_x, 4 + offset : 4 + offset + extent_y, 4 : 4 + extent_z]
            + padded[:, 4 : 4 + extent_x, 4 - offset : 4 - offset + extent_y, 4 : 4 + extent_z]
        )
        along_z = (
            padded[:, 4 : 4 + extent_x, 4 : 4 + extent_y, 4 + offset : 4 + offset + extent_z]
            + padded[:, 4 : 4 + extent_x, 4 : 4 + extent_y, 4 - offset : 4 - offset + extent_z]
        )
        summed = (
            summed
            + COEFFICIENTS[offset] * along_x
            + COEFFICIENTS[offset] * along_y
            + COEFFICIENTS[offset] * along_z
        )
    return summed


def inner_product(first_field, second_field):
    return jnp.sum(first_field * second_field, axis=(1, 2, 3))


def expand(vector):
    return vector[:, None, None, None]


def chain(occupied, potential, shifts, source_term, flip=False, first_blocks=None):
    local_bands, width_x, width_y, width_z = source_term.shape
    local_occupied = occupied.shape[0]
    band_count = lax.axis_size("band")
    local_cells = width_x * width_y * width_z
    weight_scale = 2.0 / math.sqrt(
        local_occupied * band_count * local_cells * lax.axis_size("grid")
    )
    occupied_rows = occupied.reshape(local_occupied, local_cells)
    solution = jnp.zeros_like(source_term)
    residual = source_term
    direction = source_term
    norm_now = grid_sum(inner_product(source_term, source_term), "grid")
    for iteration in range(ITERS):
        own_potential, direction = lax.optimization_barrier((potential, direction))
        potential_shift = own_potential[None] + shifts[:, None, None, None]
        padded = with_halo(direction.astype(jnp.bfloat16), (("grid", 1),), 4).astype(
            direction.dtype
        )
        padded = jnp.pad(padded, ((0, 0), (0, 0), (4, 4), (4, 4)))
        kinetic = -0.5 * second_sum(padded, width_x, width_y, width_z)
        rounded = direction.astype(jnp.bfloat16).reshape(local_bands, local_cells)
        order = sorted(range(1, band_count), key=lambda d: (min(d, band_count - d), d if flip else -d))
        if iteration == 0 and first_blocks is not None:
            blocks = first_blocks
        else:
            arrived = {
                d: lax.ppermute(rounded, "band", [(i, (i + d) % band_count) for i in range(band_count)])
                for d in order
            }
            blocks = [rounded] + [arrived[d] for d in range(1, band_count)]
        gathered = jnp.concatenate(blocks, axis=0)
        partial_margin = lax.dot_general(
            occupied_rows, gathered, (((1,), (1,)), ((), ())), preferred_element_type=jnp.float32
        )
        margins = grid_sum(partial_margin, "grid")
        scaled = (margins * weight_scale).astype(jnp.bfloat16)
        terms = lax.dot_general(
            scaled, occupied_rows, (((0,), (0,)), ((), ())), preferred_element_type=jnp.float32
        ).astype(jnp.bfloat16)
        projected = terms[:local_bands].astype(jnp.float32)
        for d in order:
            part = terms[d * local_bands : (d + 1) * local_bands]
            back = lax.ppermute(part, "band", [((i + d) % band_count, i) for i in range(band_count)])
            projected = projected + back.astype(jnp.float32)
        applied = kinetic + potential_shift * direction + projected.reshape(direction.shape)
        curvature = grid_sum(inner_product(direction, applied), "grid")
        step_size = norm_now / curvature
        if iteration + 1 == ITERS:
            return (solution, residual, direction, applied, step_size)
        solution = solution + expand(step_size) * direction
        residual = residual - expand(step_size) * applied
        if iteration + 1 < ITERS:
            norm_next = grid_sum(inner_product(residual, residual), "grid")
            direction = residual + expand(norm_next / norm_now) * direction
            norm_now = norm_next
    return (solution, residual)


def body(occupied, potential, shifts, source_term):
    pieces = 2 if source_term.shape[0] % 2 == 0 else 1
    width = source_term.shape[0] // pieces
    band_count = lax.axis_size("band")
    rounded = source_term.astype(jnp.bfloat16).reshape(source_term.shape[0], -1)
    order = sorted(range(1, band_count), key=lambda d: (min(d, band_count - d), -d))
    arrived = {
        d: lax.ppermute(rounded, "band", [(i, (i + d) % band_count) for i in range(band_count)])
        for d in order
    }
    source_blocks = [rounded] + [arrived[d] for d in range(1, band_count)]
    results = [
        chain(
            occupied,
            potential,
            shifts[k * width : (k + 1) * width],
            source_term[k * width : (k + 1) * width],
            k % 2 == 1,
            [block[k * width : (k + 1) * width] for block in source_blocks],
        )
        for k in range(pieces)
    ]
    solution, residual, direction, applied, step_size = (
        jnp.concatenate([r[i] for r in results], axis=0) for i in range(5)
    )
    return (solution + expand(step_size) * direction, residual - expand(step_size) * applied)


def solution(mesh):
    in_specs = (
        P("band", "grid", None, None),
        P("grid", None, None),
        P("band"),
        P("band", "grid", None, None),
    )
    out_specs = (P("band", "grid", None, None), P("band", "grid", None, None))
    return jax.shard_map(body, mesh=mesh, in_specs=in_specs, out_specs=out_specs, check_vma=False)
```
